256 devices in a mesh: row: 32 (over z, x_lo, core), col: 8 (over y, x_hi).
Axes of the slice: x: 4 (x_hi: 2, x_lo: 2; x = x_hi * 2 + x_lo), y: 4, z: 8, core: 2. Of those that a mesh axis runs over, the one named last changes fastest.
Arguments:
- grad_out: bfloat16 [4096, 8192], P('row', 'col'), may hold values from -6 to 6
- weight: bfloat16 [28672, 8192], P('row', 'col'), may hold values from -0.0625 to 0.0625
Outputs:
- grad_in: bfloat16 [4096, 28672], P('col', 'row')
The draws below stay inside these ranges and needn't reach their ends.
All inputs are finite; a program needn't handle non-finite values.
Results may differ from the reference program's by a relative error of at most 0.015.
Values may be sent and summed in bfloat16 or wider, within the bound.
No kernel may reach another device: no remote copies, remote signals or barrier semaphores. Data moves between devices by JAX's collectives and lax.ppermute only.
A program may use at most 128 MiB of HBM per device.

```python
import jax
import jax.numpy as jnp
from jax import lax

D = 8192
FF = 28672
TOKENS = 4096
N_COL = 8


def spiked(result, key, source, target, parts, factor):
    def block_of(position):
        return (jnp.arange(result.shape[position]) // (result.shape[position] // parts)).reshape((-1,) + (1,) * (result.ndim - 1 - position))

    near = jax.random.permutation(key, parts)[block_of(target)]
    far = (block_of(target) + parts // 2) % parts
    return jnp.where((block_of(source) == near) | (block_of(source) == far), factor * result, result)


def block_scale(key, dims, pieces, smallest, largest):
    def one(dim, blocks):
        steps = jax.random.uniform(jax.random.fold_in(jax.random.fold_in(key, 6), dim), (blocks,), jnp.float32, smallest / len(pieces), largest / len(pieces))
        return jnp.repeat(jnp.exp(steps), dims[dim] // blocks).reshape((-1,) + (1,) * (len(dims) - dim - 1))

    factor_of = one(*pieces[0])
    for cut in pieces[1:]:
        factor_of = factor_of * one(*cut)
    return factor_of


def bell_draw(key, extent, spread, bound, shards=(), kind=jnp.bfloat16):
    gain = block_scale(key, extent, shards, -0.22, 0.18) if shards else 1.0
    entries = jax.random.normal(key, extent, jnp.float32) * spread * gain
    return jnp.minimum(jnp.maximum(entries, -bound), bound).astype(kind)


def noise_with(key, dims, spread, most, pieces, heavy, dtype=jnp.bfloat16):
    drawn = spread * jax.random.normal(key, dims, jnp.float32)
    if pieces:
        drawn = drawn * block_scale(key, dims, pieces, -0.22, 0.18)
    return jnp.clip(spiked(drawn, jax.random.fold_in(key, 3), *heavy), -most, most).astype(dtype)


def setup_inputs(seed: int = 0) -> dict:
    key_list = jax.random.split(jax.random.key(seed), 3)
    return {
        "grad_out": noise_with(key_list[0], (TOKENS, D), 1.0, 6.0, ((0, 32), (1, 8)), (1, 0, 32, 2.75)),
        "weight": bell_draw(key_list[1], (FF, D), D ** -0.5, 0.0625, ((0, 32), (1, 8))),
    }


def reference(grad_out, weight):
    width = D // N_COL
    total = jnp.zeros((grad_out.shape[0], weight.shape[0]), jnp.float32)
    for block in range(N_COL):
        left = grad_out[:, block * width:(block + 1) * width]
        right = weight[:, block * width:(block + 1) * width]
        piece = jnp.dot(left, right.T, preferred_element_type=jnp.float32)
        rounded = lax.optimization_barrier(piece.astype(jnp.bfloat16))
        total = total + rounded.astype(jnp.float32)
    return total.astype(jnp.bfloat16)
```

```python
import jax
import jax.numpy as jnp
from jax import lax
from jax.sharding import PartitionSpec as P


def contract_last(left_side, right_side):
    return lax.dot_general(
        left_side, right_side, (((1,), (1,)), ((), ())), preferred_element_type=jnp.float32
    )


def body(grad_out, weight):
    n_col = lax.axis_size("col")
    gathered = lax.all_gather(grad_out, "row", axis=0, tiled=True)
    rounded = contract_last(gathered, weight).astype(jnp.bfloat16)
    blocks = rounded.reshape(n_col, rounded.shape[0] // n_col, rounded.shape[1])
    received = lax.all_to_all(blocks, "col", 0, 0, tiled=True)
    return received.astype(jnp.float32).sum(0).astype(jnp.bfloat16)


def solution(mesh):
    in_specs = (P("row", "col"), P("row", "col"))
    out_specs = P("col", "row")
    return jax.shard_map(body, mesh=mesh, in_specs=in_specs, out_specs=out_specs, check_vma=False)
```

```python
import jax
import jax.numpy as jnp
from jax import lax
from jax.sharding import Mesh, PartitionSpec as P


def contract_last(left_side, right_side):
    return lax.dot_general(
        left_side, right_side, (((1,), (1,)), ((), ())), preferred_element_type=jnp.float32
    )


def body(grad_out, weight):
    n_col = lax.axis_size("col")
    n_core = lax.axis_size("core")
    both = lax.all_gather(weight, "core", axis=0, tiled=True)
    gathered = lax.all_gather(grad_out, "rz", axis=0, tiled=True)
    rounded = contract_last(gathered, both).astype(jnp.bfloat16)
    blocks = rounded.reshape(n_col, rounded.shape[0] // n_col, rounded.shape[1])
    received = lax.all_to_all(blocks, "col", 0, 0, tiled=True)
    summed = received.astype(jnp.float32).sum(0).astype(jnp.bfloat16)
    rows, width = summed.shape[0], weight.shape[0]
    by_owner = summed.reshape(rows, n_core, width).transpose(1, 0, 2)
    mine = lax.all_to_all(by_owner, "core", 0, 0, tiled=True)
    per_row = grad_out.shape[0]
    mine = mine.reshape(n_core, rows // per_row, per_row, width).transpose(1, 0, 2, 3)
    return mine.reshape(-1, width)


def solution(mesh):
    n_row, n_col = mesh.devices.shape
    fine = Mesh(mesh.devices.reshape(n_row // 2, 2, n_col), ("rz", "core", "col"))
    in_specs = (P(("rz", "core"), "col"), P(("rz", "core"), "col"))
    out_specs = P("col", ("rz", "core"))
    return jax.shard_map(body, mesh=fine, in_specs=in_specs, out_specs=out_specs, check_vma=False)
```

```python
import jax
import jax.numpy as jnp
from jax import lax
from jax.sharding import PartitionSpec as P


def contract_last(left_side, right_side):
    return lax.dot_general(
        left_side, right_side, (((1,), (1,)), ((), ())), preferred_element_type=jnp.float32
    )


def body(grad_out, weight):
    n_col = lax.axis_size("col")
    gathered = lax.all_gather(grad_out, "row", axis=0, tiled=True)
    me = lax.axis_index("col")
    rows = gathered.shape[0] // n_col

    def block_for(dest):
        left = lax.dynamic_slice_in_dim(gathered, dest * rows, rows, 0)
        return contract_last(left, weight).astype(jnp.bfloat16)

    total = block_for(me).astype(jnp.float32)
    for shift in range(1, n_col):
        ring = [(i, (i + shift) % n_col) for i in range(n_col)]
        arrived = lax.ppermute(block_for((me + shift) % n_col), "col", ring)
        total = total + arrived.astype(jnp.float32)
    return total.astype(jnp.bfloat16)


def solution(mesh):
    in_specs = (P("row", "col"), P("row", "col"))
    out_specs = P("col", "row")
    return jax.shard_map(body, mesh=mesh, in_specs=in_specs, out_specs=out_specs, check_vma=False)
```

```python
import jax
import jax.numpy as jnp
from jax import lax
from jax.sharding import PartitionSpec as P


def contract_last(left_side, right_side):
    return lax.dot_general(
        left_side, right_side, (((1,), (1,)), ((), ())), preferred_element_type=jnp.float32
    )


def body(grad_out, weight):
    n_col = lax.axis_size("col")
    gathered = lax.all_gather(grad_out, "row", axis=0, tiled=True)
    me = lax.axis_index("col")
    rows = gathered.shape[0] // n_col

    def block_for(dest):
        left = lax.dynamic_slice_in_dim(gathered, dest * rows, rows, 0)
        return contract_last(left, weight).astype(jnp.bfloat16)

    total = block_for(me).astype(jnp.float32)
    for shift in range(1, n_col):
        ring = [(i, (i + shift) % n_col) for i in range(n_col)]
        arrived = lax.ppermute(block_for((me + shift) % n_col), "col", ring)
        total = lax.optimization_barrier(total + arrived.astype(jnp.float32))
    return total.astype(jnp.bfloat16)


def solution(mesh):
    in_specs = (P("row", "col"), P("row", "col"))
    out_specs = P("col", "row")
    return jax.shard_map(body, mesh=mesh, in_specs=in_specs, out_specs=out_specs, check_vma=False)
```

```python
import jax
import jax.numpy as jnp
from jax import lax
from jax.sharding import PartitionSpec as P


def contract_last(left_side, right_side):
    return lax.dot_general(
        left_side, right_side, (((1,), (1,)), ((), ())), preferred_element_type=jnp.float32
    )


def body(grad_out, weight):
    n_col = lax.axis_size("col")
    gathered = lax.all_gather(grad_out, "row", axis=0, tiled=True)
    me = lax.axis_index("col")
    rows = gathered.shape[0] // n_col

    def block_for(dest):
        left = lax.dynamic_slice_in_dim(gathered, dest * rows, rows, 0)
        return contract_last(left, weight).astype(jnp.bfloat16)

    n_y = n_col // 2

    def dest(i, dy, dx):
        return ((i // 2 + dy) % n_y) * 2 + (i % 2 + dx) % 2

    offsets = [(n_y // 2, 1), (1, 1), (n_y - 1, 1), (0, 1), (n_y // 2, 0), (1, 0), (n_y - 1, 0)]
    total = block_for(me).astype(jnp.float32)
    for dy, dx in offsets:
        ring = [(i, dest(i, dy, dx)) for i in range(n_col)]
        arrived = lax.ppermute(block_for(dest(me, dy, dx)), "col", ring)
        total = lax.optimization_barrier(total + arrived.astype(jnp.float32))
    return total.astype(jnp.bfloat16)


def solution(mesh):
    in_specs = (P("row", "col"), P("row", "col"))
    out_specs = P("col", "row")
    return jax.shard_map(body, mesh=mesh, in_specs=in_specs, out_specs=out_specs, check_vma=False)
```

```python
import jax
import jax.numpy as jnp
from jax import lax
from jax.sharding import PartitionSpec as P


def contract_last(left_side, right_side):
    return lax.dot_general(
        left_side, right_side, (((1,), (1,)), ((), ())), preferred_element_type=jnp.float32
    )


def body(grad_out, weight):
    n_col = lax.axis_size("col")
    gathered = lax.all_gather(grad_out, "row", axis=0, tiled=True)
    me = lax.axis_index("col")
    rows = gathered.shape[0] // n_col

    def block_for(dest):
        left = lax.dynamic_slice_in_dim(gathered, dest * rows, rows, 0)
        return contract_last(left, weight).astype(jnp.bfloat16)

    n_y = n_col // 2

    def dest(i, dy, dx):
        return ((i // 2 + dy) % n_y) * 2 + (i % 2 + dx) % 2

    offsets = [(n_y // 2, 1), (n_y // 2, 0), (1, 1), (1, 0), (n_y - 1, 1), (n_y - 1, 0), (0, 1)]
    total = block_for(me).astype(jnp.float32)
    for dy, dx in offsets:
        ring = [(i, dest(i, dy, dx)) for i in range(n_col)]
        arrived = lax.ppermute(block_for(dest(me, dy, dx)), "col", ring)
        total = lax.optimization_barrier(total + arrived.astype(jnp.float32))
    return total.astype(jnp.bfloat16)


def solution(mesh):
    in_specs = (P("row", "col"), P("row", "col"))
    out_specs = P("col", "row")
    return jax.shard_map(body, mesh=mesh, in_specs=in_specs, out_specs=out_specs, check_vma=False)
```
